512 devices in a mesh: row: 32 (over z_hi, y), col: 16 (over x, z_lo, core).
Axes of the slice: x: 4, y: 8, z: 8 (z_hi: 4, z_lo: 2; z = z_hi * 2 + z_lo), core: 2. Of those that a mesh axis runs over, the one named last changes fastest.
Arguments:
- s_rows: bfloat16 [32768, 1024], P('row', 'col'), may hold values from -0.1875 to 0.1875
- iterate: bfloat16 [1024, 32768], P('row', 'col'), may hold values from -6 to 6
Outputs:
- product: bfloat16 [32768, 32768], P('row', 'col')
The draws below stay inside these ranges and needn't reach their ends.
All inputs are finite; a program needn't handle non-finite values.
Results may differ from the reference program's by a relative error of at most 0.001.
Values may be sent and summed in bfloat16 or wider, within the bound.
No kernel may reach another device: no remote copies, remote signals or barrier semaphores. Data moves between devices by JAX's collectives and lax.ppermute only.
A program may use at most 64 MiB of HBM per device.

```python
import jax
import jax.numpy as jnp
from jax import lax

N = 32768
M = 32768
K = 1024


def level_of(own_key, shape, cuts, low, high):
    factor_of, own = 1.0, jax.random.fold_in(own_key, 6)
    for axis_at, shards_of in cuts:
        steps = jnp.exp(jax.random.uniform(jax.random.fold_in(own, axis_at), (shards_of,), jnp.float32, low / len(cuts), high / len(cuts)))
        factor_of = factor_of * jnp.repeat(steps, shape[axis_at] // shards_of).reshape([-1 if axis == axis_at else 1 for axis in range(len(shape))])
    return factor_of


def noise(stream_key, dims, scale, limit, pieces=(), held_as=jnp.bfloat16):
    level = level_of(stream_key, dims, pieces, -0.22, 0.18) if pieces else 1.0
    values = jax.random.normal(stream_key, dims, jnp.float32) * scale * level
    return jnp.minimum(jnp.maximum(values, -limit), limit).astype(held_as)


def setup_inputs(seed: int = 0) -> dict:
    seeds = jax.random.split(jax.random.key(seed), 3)
    return {
        "s_rows": noise(seeds[0], (M, K), K ** -0.5, 0.1875, ((0, 32), (1, 16))),
        "iterate": noise(seeds[1], (K, N), 1.0, 6.0, ((0, 32), (1, 16))),
    }


def reference(s_rows, iterate):
    total = jnp.dot(s_rows.astype(jnp.float32), iterate.astype(jnp.float32), precision=lax.Precision.HIGHEST, preferred_element_type=jnp.float32)
    return total.astype(jnp.bfloat16)
```

```python
import jax
import jax.numpy as jnp
from jax import lax
from jax.sharding import Mesh, PartitionSpec as P

ROW = ("z_hi", "y")
COL = ("x", "z_lo", "core")


def shards(s_rows, iterate):
    panel = lax.all_gather(s_rows, COL, axis=1, tiled=True)
    nz, ny = lax.axis_size("z_hi"), lax.axis_size("y")
    w = lax.all_gather(iterate, "z_hi", axis=0, tiled=False)
    w = lax.all_gather(w, "y", axis=0, tiled=False)
    s4 = panel.reshape(panel.shape[0], nz, ny, -1)
    product = jnp.einsum("rzyk,yzkc->rc", s4, w, preferred_element_type=jnp.float32)
    return product.astype(jnp.bfloat16)


def solution(mesh):
    nr, nc = mesh.devices.shape
    devs = mesh.devices.reshape(4, nr // 4, nc // 4, 2, 2)
    m = Mesh(devs, ROW + COL)
    return jax.shard_map(shards, mesh=m, in_specs=(P(ROW, COL), P(ROW, COL)), out_specs=P(ROW, COL), check_vma=False)
```

```python
import jax
import jax.numpy as jnp
from jax import lax
from jax.sharding import Mesh, PartitionSpec as P

ROW = ("z_hi", "y")
COL = ("x", "z_lo", "core")


def swap(a, axis, cat):
    o = lax.ppermute(a, axis, [(0, 1), (1, 0)])
    first = lax.axis_index(axis) == 0
    return jnp.where(first, jnp.concatenate([a, o], cat), jnp.concatenate([o, a], cat))


def ring(a, axis, n):
    parts = [a] + [lax.ppermute(a, axis, [(i, (i - d) % n) for i in range(n)]) for d in range(1, n)]
    return jnp.roll(jnp.stack(parts), lax.axis_index(axis), axis=0)


def GZ(a):
    return lax.all_gather(a, "z_hi", axis=0, tiled=False)


def shards(s_rows, iterate):
    nx, nz, ny = lax.axis_size("x"), lax.axis_size("z_hi"), lax.axis_size("y")
    s = swap(s_rows, "core", 1)
    s = swap(s, "z_lo", 1)
    s = ring(s, "x", nx)
    w = GZ(iterate)
    w = lax.all_gather(w, "y", axis=0, tiled=False)
    s4 = s.reshape(nx, s.shape[1], ny, -1)
    product = jnp.einsum("zryk,yzkc->rc", s4, w, preferred_element_type=jnp.float32)
    return product.astype(jnp.bfloat16)


def solution(mesh):
    nr, nc = mesh.devices.shape
    devs = mesh.devices.reshape(4, nr // 4, nc // 4, 2, 2)
    m = Mesh(devs, ROW + COL)
    return jax.shard_map(shards, mesh=m, in_specs=(P(ROW, COL), P(ROW, COL)), out_specs=P(ROW, COL), check_vma=False)
```

```python
import jax
import jax.numpy as jnp
from jax import lax
from jax.experimental import pallas as pl
from jax.experimental.pallas import tpu as pltpu
from jax.sharding import Mesh, PartitionSpec as P

ROW = ("z_hi", "y")
COL = ("x", "z_lo", "core")


def swap(a, axis, cat):
    o = lax.ppermute(a, axis, [(0, 1), (1, 0)])
    first = lax.axis_index(axis) == 0
    return jnp.where(first, jnp.concatenate([a, o], cat), jnp.concatenate([o, a], cat))


def ring(a, axis, n):
    parts = [a] + [lax.ppermute(a, axis, [(i, (i - d) % n) for i in range(n)]) for d in range(1, n)]
    return jnp.roll(jnp.stack(parts), lax.axis_index(axis), axis=0)


def GZ(a):
    return lax.all_gather(a, "z_hi", axis=0, tiled=False)


def mm_kernel(a_ref, b_ref, o_ref):
    o_ref[...] = jnp.dot(a_ref[...], b_ref[...], preferred_element_type=jnp.float32).astype(o_ref.dtype)


def matmul(a, b, tm=1024, tn=512):
    m, k = a.shape
    n = b.shape[1]
    return pl.pallas_call(
        mm_kernel,
        out_shape=jax.ShapeDtypeStruct((m, n), jnp.bfloat16),
        grid=(n // tn, m // tm),
        in_specs=[pl.BlockSpec((tm, k), lambda j, i: (i, 0)), pl.BlockSpec((k, tn), lambda j, i: (0, j))],
        out_specs=pl.BlockSpec((tm, tn), lambda j, i: (i, j)),
        compiler_params=pltpu.CompilerParams(vmem_limit_bytes=48 * 1024 * 1024),
        cost_estimate=pl.CostEstimate(flops=2 * m * n * k, bytes_accessed=2 * (m * k + k * n + m * n), transcendentals=0),
    )(a, b)


def shards(s_rows, iterate):
    nx, nz, ny = lax.axis_size("x"), lax.axis_size("z_hi"), lax.axis_size("y")
    s = swap(s_rows, "core", 1)
    s = swap(s, "z_lo", 1)
    s = ring(s, "x", nx)
    w = GZ(iterate)
    w = lax.all_gather(w, "y", axis=0, tiled=False)
    R = s.shape[1]
    panel = jnp.transpose(s.reshape(nx, R, ny, -1), (1, 2, 0, 3)).reshape(R, -1)
    return matmul(panel, w.reshape(-1, w.shape[-1]))


def solution(mesh):
    nr, nc = mesh.devices.shape
    devs = mesh.devices.reshape(4, nr // 4, nc // 4, 2, 2)
    m = Mesh(devs, ROW + COL)
    return jax.shard_map(shards, mesh=m, in_specs=(P(ROW, COL), P(ROW, COL)), out_specs=P(ROW, COL), check_vma=False)
```

```python
import jax
import jax.numpy as jnp
from jax import lax
from jax.experimental import pallas as pl
from jax.experimental.pallas import tpu as pltpu
from jax.sharding import Mesh, PartitionSpec as P

ROW = ("z_hi", "y")
COL = ("x", "z_lo", "core")


def swap(a, axis, cat):
    o = lax.ppermute(a, axis, [(0, 1), (1, 0)])
    first = lax.axis_index(axis) == 0
    return jnp.where(first, jnp.concatenate([a, o], cat), jnp.concatenate([o, a], cat))


def ring(a, axis, n):
    parts = [a] + [lax.ppermute(a, axis, [(i, (i - d) % n) for i in range(n)]) for d in range(1, n)]
    return jnp.roll(jnp.stack(parts), lax.axis_index(axis), axis=0)


def GZ(a):
    return lax.all_gather(a, "z_hi", axis=0, tiled=False)


def mm_kernel(a_ref, b_ref, o_ref):
    o_ref[...] = jnp.dot(a_ref[...], b_ref[...], preferred_element_type=jnp.float32).astype(o_ref.dtype)


def matmul(a, b, tm=1024, tn=256):
    m, k = a.shape
    n = b.shape[1]
    return pl.pallas_call(
        mm_kernel,
        out_shape=jax.ShapeDtypeStruct((m, n), jnp.bfloat16),
        grid=(n // tn, m // tm),
        in_specs=[pl.BlockSpec((tm, k), lambda j, i: (i, 0)), pl.BlockSpec((k, tn), lambda j, i: (0, j))],
        out_specs=pl.BlockSpec((tm, tn), lambda j, i: (i, j)),
        compiler_params=pltpu.CompilerParams(vmem_limit_bytes=48 * 1024 * 1024),
        cost_estimate=pl.CostEstimate(flops=2 * m * n * k, bytes_accessed=2 * (m * k + k * n + m * n), transcendentals=0),
    )(a, b)


def shards(s_rows, iterate):
    nx, nz, ny = lax.axis_size("x"), lax.axis_size("z_hi"), lax.axis_size("y")
    s = swap(s_rows, "core", 1)
    s = swap(s, "z_lo", 1)
    s = ring(s, "x", nx)
    w = GZ(iterate)
    w = lax.all_gather(w, "y", axis=0, tiled=False)
    R = s.shape[1]
    panel = jnp.transpose(s.reshape(nx, R, ny, -1), (1, 2, 0, 3)).reshape(R, -1)
    return matmul(panel, w.reshape(-1, w.shape[-1]))


def solution(mesh):
    nr, nc = mesh.devices.shape
    devs = mesh.devices.reshape(4, nr // 4, nc // 4, 2, 2)
    m = Mesh(devs, ROW + COL)
    return jax.shard_map(shards, mesh=m, in_specs=(P(ROW, COL), P(ROW, COL)), out_specs=P(ROW, COL), check_vma=False)
```

```python
import jax
import jax.numpy as jnp
from jax import lax
from jax.experimental import pallas as pl
from jax.experimental.pallas import tpu as pltpu
from jax.sharding import Mesh, PartitionSpec as P

ROW = ("z_hi", "y")
COL = ("x", "z_lo", "core")


def swap(a, axis, cat):
    o = lax.ppermute(a, axis, [(0, 1), (1, 0)])
    first = lax.axis_index(axis) == 0
    return jnp.where(first, jnp.concatenate([a, o], cat), jnp.concatenate([o, a], cat))


def ring(a, axis, n):
    parts = [a] + [lax.ppermute(a, axis, [(i, (i - d) % n) for i in range(n)]) for d in range(1, n)]
    return jnp.roll(jnp.stack(parts), lax.axis_index(axis), axis=0)


def GZ(a):
    return lax.all_gather(a, "z_hi", axis=0, tiled=False)


def mm_kernel(a_ref, b_ref, o_ref):
    o_ref[...] = jnp.dot(a_ref[...], b_ref[...], preferred_element_type=jnp.float32).astype(o_ref.dtype)


def matmul(a, b, tm=1024, tn=1024):
    m, k = a.shape
    n = b.shape[1]
    return pl.pallas_call(
        mm_kernel,
        out_shape=jax.ShapeDtypeStruct((m, n), jnp.bfloat16),
        grid=(n // tn, m // tm),
        in_specs=[pl.BlockSpec((tm, k), lambda j, i: (i, 0)), pl.BlockSpec((k, tn), lambda j, i: (0, j))],
        out_specs=pl.BlockSpec((tm, tn), lambda j, i: (i, j)),
        compiler_params=pltpu.CompilerParams(vmem_limit_bytes=48 * 1024 * 1024),
        cost_estimate=pl.CostEstimate(flops=2 * m * n * k, bytes_accessed=2 * (m * k + k * n + m * n), transcendentals=0),
    )(a, b)


def shards(s_rows, iterate):
    nx, nz, ny = lax.axis_size("x"), lax.axis_size("z_hi"), lax.axis_size("y")
    s = swap(s_rows, "core", 1)
    s = swap(s, "z_lo", 1)
    s = ring(s, "x", nx)
    w = GZ(iterate)
    w = lax.all_gather(w, "y", axis=0, tiled=False)
    R = s.shape[1]
    panel = jnp.transpose(s.reshape(nx, R, ny, -1), (1, 2, 0, 3)).reshape(R, -1)
    return matmul(panel, w.reshape(-1, w.shape[-1]))


def solution(mesh):
    nr, nc = mesh.devices.shape
    devs = mesh.devices.reshape(4, nr // 4, nc // 4, 2, 2)
    m = Mesh(devs, ROW + COL)
    return jax.shard_map(shards, mesh=m, in_specs=(P(ROW, COL), P(ROW, COL)), out_specs=P(ROW, COL), check_vma=False)
```

```python
import jax
import jax.numpy as jnp
from jax import lax
from jax.experimental import pallas as pl
from jax.experimental.pallas import tpu as pltpu
from jax.sharding import Mesh, PartitionSpec as P

ROW = ("z_hi", "y")
COL = ("x", "z_lo", "core")


def swap(a, axis, cat):
    o = lax.ppermute(a, axis, [(0, 1), (1, 0)])
    first = lax.axis_index(axis) == 0
    return jnp.where(first, jnp.concatenate([a, o], cat), jnp.concatenate([o, a], cat))


def ring(a, axis, n):
    parts = [a] + [lax.ppermute(a, axis, [(i, (i - d) % n) for i in range(n)]) for d in range(1, n)]
    return jnp.roll(jnp.stack(parts), lax.axis_index(axis), axis=0)


def GZ(a):
    return lax.all_gather(a, "z_hi", axis=0, tiled=False)


def mm_kernel(a_ref, b_ref, o_ref):
    o_ref[...] = jnp.dot(a_ref[...], b_ref[...], preferred_element_type=jnp.float32).astype(o_ref.dtype)


def matmul(a, b, tm=512, tn=2048):
    m, k = a.shape
    n = b.shape[1]
    return pl.pallas_call(
        mm_kernel,
        out_shape=jax.ShapeDtypeStruct((m, n), jnp.bfloat16),
        grid=(n // tn, m // tm),
        in_specs=[pl.BlockSpec((tm, k), lambda j, i: (i, 0)), pl.BlockSpec((k, tn), lambda j, i: (0, j))],
        out_specs=pl.BlockSpec((tm, tn), lambda j, i: (i, j)),
        compiler_params=pltpu.CompilerParams(vmem_limit_bytes=48 * 1024 * 1024),
        cost_estimate=pl.CostEstimate(flops=2 * m * n * k, bytes_accessed=2 * (m * k + k * n + m * n), transcendentals=0),
    )(a, b)


def shards(s_rows, iterate):
    nx, nz, ny = lax.axis_size("x"), lax.axis_size("z_hi"), lax.axis_size("y")
    s = swap(s_rows, "core", 1)
    s = swap(s, "z_lo", 1)
    s = ring(s, "x", nx)
    w = GZ(iterate)
    w = lax.all_gather(w, "y", axis=0, tiled=False)
    R = s.shape[1]
    panel = jnp.transpose(s.reshape(nx, R, ny, -1), (1, 2, 0, 3)).reshape(R, -1)
    return matmul(panel, w.reshape(-1, w.shape[-1]))


def solution(mesh):
    nr, nc = mesh.devices.shape
    devs = mesh.devices.reshape(4, nr // 4, nc // 4, 2, 2)
    m = Mesh(devs, ROW + COL)
    return jax.shard_map(shards, mesh=m, in_specs=(P(ROW, COL), P(ROW, COL)), out_specs=P(ROW, COL), check_vma=False)
```
